32 devices in a mesh: dp: 8 (over z, core), tensor: 4 (over y, x).
Axes of the slice: x: 2, y: 2, z: 4, core: 2. Of those that a mesh axis runs over, the one named last changes fastest.
Arguments:
- tokens: bfloat16 [512, 8192], P(None, 'dp'), may hold values from -6 to 6
- w_gate_up: bfloat16 [8192, 2, 28672], P('dp', None, 'tensor'), may hold values from -0.0625 to 0.0625
- w_down: bfloat16 [28672, 8192], P('tensor', 'dp'), may hold values from -0.03125 to 0.03125
- targets: bfloat16 [512, 8192], P(None, 'dp'), may hold values from -3 to 3
- proj_model: bfloat16 [8192, 128], P('dp'), may hold values from -0.0625 to 0.0625
- proj_hidden: bfloat16 [28672, 192], P('tensor'), may hold values from -0.03125 to 0.03125
- store: bfloat16 [4096, 12288], P(('dp', 'tensor')), may hold values from -0.017944336 to 0.017944336
Outputs:
- scores: float32 [4, 4096], P(None, ('dp', 'tensor'))
The draws below stay inside these ranges and needn't reach their ends.
All inputs are finite; a program needn't handle non-finite values.
Results may differ from the reference program's by a relative error of at most 0.02.
Values may be sent and summed in bfloat16 or wider, within the bound.
No kernel may reach another device: no remote copies, remote signals or barrier semaphores. Data moves between devices by JAX's collectives and lax.ppermute only.
A program may use at most 256 MiB of HBM per device.

```python
import jax
import jax.numpy as jnp
from jax import lax

D = 8192
FF = 28672
RANK = 64
SEQ = 128
TOKENS = 512
EXAMPLES = 4096


def strengthened(values, stream_key, source, target, shards_of, factor):
    owner, partner = [(jnp.arange(values.shape[position]) // (values.shape[position] // shards_of)).reshape([-1 if axis == position else 1 for axis in range(values.ndim)]) for position in (source, target)]
    chosen = jax.random.permutation(stream_key, shards_of)[partner]
    strong = (owner == chosen) | (owner == (partner + shards_of // 2) % shards_of)
    return jnp.where(strong, factor * values, values)


def level_of(key, extent, pieces, low, high):
    factor_of = 1.0
    for dim, parts in pieces:
        steps = jax.random.uniform(jax.random.fold_in(jax.random.fold_in(key, 6), dim), (parts,), jnp.float32, low / len(pieces), high / len(pieces))
        factor_of = factor_of * jnp.repeat(jnp.exp(steps), extent[dim] // parts).reshape((-1,) + (1,) * (len(extent) - 1 - dim))
    return factor_of


def noise(key, shape, scale, reach, shards=(), dtype=jnp.bfloat16):
    gain = level_of(key, shape, shards, -0.22, 0.18) if shards else 1.0
    values = jax.random.normal(key, shape, jnp.float32) * scale * gain
    return jnp.minimum(jnp.maximum(values, -reach), reach).astype(dtype)


def heavy_noise(own_key, extent, width, bound, shards, heavy, held_as=jnp.bfloat16):
    values = width * jax.random.normal(own_key, extent, jnp.float32)
    if shards:
        values = values * level_of(own_key, extent, shards, -0.22, 0.18)
    return jnp.clip(strengthened(values, jax.random.fold_in(own_key, 3), *heavy), -bound, bound).astype(held_as)


def setup_inputs(seed: int = 0) -> dict:
    streams_of = jax.random.split(jax.random.key(seed), 8)
    tokens = heavy_noise(streams_of[0], (TOKENS, D), 1.0, 6.0, ((1, 8),), (1, 0, 8, 2.0))
    w_gate_up = noise(streams_of[1], (D, 2, FF), D ** -0.5, 0.0625, ((0, 8), (2, 4)))
    w_down = noise(streams_of[2], (FF, D), FF ** -0.5, 0.03125, ((0, 4), (1, 8)))
    targets = noise(streams_of[3], (TOKENS, D), 0.5, 3.0, ((1, 8),))
    proj_model = noise(streams_of[4], (D, 2 * RANK), D ** -0.5, 0.0625, ((0, 8),))
    proj_hidden = noise(streams_of[5], (FF, 3 * RANK), FF ** -0.5, 0.03125, ((0, 4),))
    store = noise(streams_of[6], (EXAMPLES, 3 * RANK * RANK), 0.003, 0.017944336, ((0, 32),))
    return dict(tokens=tokens, w_gate_up=w_gate_up, w_down=w_down, targets=targets, proj_model=proj_model, proj_hidden=proj_hidden, store=store)


def reference(tokens, w_gate_up, w_down, targets, proj_model, proj_hidden, store):
    gate = jnp.dot(tokens, w_gate_up[:, 0, :], preferred_element_type=jnp.float32)
    up = jnp.dot(tokens, w_gate_up[:, 1, :], preferred_element_type=jnp.float32)
    sig = jax.nn.sigmoid(gate)
    act = gate * sig
    hidden = (act * up).astype(jnp.bfloat16)
    out = jnp.dot(hidden, w_down, preferred_element_type=jnp.float32)
    cot = (out - targets.astype(jnp.float32)).astype(jnp.bfloat16)
    grad_hidden = jnp.dot(cot, w_down.T, preferred_element_type=jnp.float32)
    dgate = (grad_hidden * up * sig * (1.0 + gate * (1.0 - sig))).astype(jnp.bfloat16)
    dup = (grad_hidden * act).astype(jnp.bfloat16)
    a_in = jnp.dot(tokens, proj_model[:, :RANK], preferred_element_type=jnp.float32)
    a_out = jnp.dot(cot, proj_model[:, RANK:], preferred_element_type=jnp.float32)
    b_gate = jnp.dot(dgate, proj_hidden[:, :RANK], preferred_element_type=jnp.float32)
    b_up = jnp.dot(dup, proj_hidden[:, RANK:2 * RANK], preferred_element_type=jnp.float32)
    b_hid = jnp.dot(hidden, proj_hidden[:, 2 * RANK:], preferred_element_type=jnp.float32)
    tests = TOKENS // SEQ
    hi = lax.Precision.HIGHEST
    g_gate = jnp.einsum('sti,stj->sij', a_in.reshape(tests, SEQ, RANK), b_gate.reshape(tests, SEQ, RANK), precision=hi)
    g_up = jnp.einsum('sti,stj->sij', a_in.reshape(tests, SEQ, RANK), b_up.reshape(tests, SEQ, RANK), precision=hi)
    g_down = jnp.einsum('sti,stj->sij', b_hid.reshape(tests, SEQ, RANK), a_out.reshape(tests, SEQ, RANK), precision=hi)
    grads = jnp.stack([g_gate, g_up, g_down], axis=1).reshape(tests, 3 * RANK * RANK)
    return jnp.dot(grads.astype(jnp.bfloat16), store.T, preferred_element_type=jnp.float32)
```

```python
import jax
import jax.numpy as jnp
import numpy as np
from jax import lax
from jax.sharding import Mesh, PartitionSpec as P

RANK = 64
SEQ = 128
CHUNKS = 8


def reduce_to_ends(part, n_z, chunks):
    z = lax.axis_index("z")
    half = part.shape[0] // 2
    rows = half // chunks
    low, high = part[:half], part[half:]
    left = [(i, i - 1) for i in range(1, n_z)]
    right = [(i, i + 1) for i in range(n_z - 1)]
    recv_l = jnp.zeros((rows,) + part.shape[1:], jnp.bfloat16)
    recv_r = recv_l
    outs_l, outs_r = [], []
    for step in range(chunks + n_z - 1):
        k_l = jnp.clip(step - (n_z - 1 - z), 0, chunks - 1)
        k_r = jnp.clip(step - z, 0, chunks - 1)
        acc_l = lax.dynamic_slice_in_dim(low, k_l * rows, rows, 0) + recv_l.astype(jnp.float32)
        acc_r = lax.dynamic_slice_in_dim(high, k_r * rows, rows, 0) + recv_r.astype(jnp.float32)
        if step >= n_z - 1:
            outs_l.append(acc_l)
            outs_r.append(acc_r)
        if step < chunks + n_z - 2:
            recv_l = lax.ppermute(acc_l.astype(jnp.bfloat16), "z", left)
            recv_r = lax.ppermute(acc_r.astype(jnp.bfloat16), "z", right)
    return jnp.concatenate(outs_l, axis=0), jnp.concatenate(outs_r, axis=0)


def bcast_from_ends(low_own, high_own, n_z, chunks):
    z = lax.axis_index("z")
    half = low_own.shape[0]
    rows = half // chunks
    left = [(i, i - 1) for i in range(1, n_z)]
    right = [(i, i + 1) for i in range(n_z - 1)]
    recv_l = jnp.zeros((rows,) + low_own.shape[1:], low_own.dtype)
    recv_r = recv_l
    got_l, got_r = [], []
    for step in range(chunks + n_z - 2):
        k = jnp.clip(step, 0, chunks - 1)
        send_l = jnp.where(z == 0, lax.dynamic_slice_in_dim(low_own, k * rows, rows, 0), recv_l)
        send_r = jnp.where(z == n_z - 1, lax.dynamic_slice_in_dim(high_own, k * rows, rows, 0), recv_r)
        recv_l = lax.ppermute(send_l, "z", right)
        recv_r = lax.ppermute(send_r, "z", left)
        got_l.append(recv_l)
        got_r.append(recv_r)
    got_l = jnp.stack(got_l)
    got_r = jnp.stack(got_r)
    start_l = jnp.clip(z - 1, 0, n_z - 2)
    start_r = jnp.clip(n_z - 2 - z, 0, n_z - 2)
    low = lax.dynamic_slice_in_dim(got_l, start_l, chunks, 0).reshape(low_own.shape)
    high = lax.dynamic_slice_in_dim(got_r, start_r, chunks, 0).reshape(high_own.shape)
    low = jnp.where(z == 0, low_own, low)
    high = jnp.where(z == n_z - 1, high_own, high)
    return jnp.concatenate([low, high], axis=0)


def local(tokens, w_gate_up, w_down, targets, proj_model, proj_hidden, store):
    n_z = lax.axis_size("z")
    n_core = lax.axis_size("core")
    z = lax.axis_index("z")
    core = lax.axis_index("core")
    total = tokens.shape[0]
    half = total // 2
    width_ff = w_down.shape[0]
    width_h = width_ff // n_core
    hi = lax.Precision.HIGHEST
    tests = total // SEQ
    chunks = CHUNKS

    a_in_part = jnp.dot(tokens, proj_model[:, :RANK], preferred_element_type=jnp.float32)

    both = jnp.einsum("td,dkf->tkf", tokens, w_gate_up, preferred_element_type=jnp.float32)
    both = both.reshape(total, 2, n_core, width_h)
    both = lax.psum_scatter(both, "core", scatter_dimension=2, tiled=False)
    low, high = reduce_to_ends(both, n_z, chunks)

    def act_of(gu):
        gate = gu[:, 0]
        up = gu[:, 1]
        sig = jax.nn.sigmoid(gate)
        act = gate * sig
        return gate, up, sig, act, (act * up).astype(jnp.bfloat16)

    g_l, u_l, s_l, a_l, h_l = act_of(low)
    g_h, u_h, s_h, a_h, h_h = act_of(high)

    hidden_half = bcast_from_ends(h_l, h_h, n_z, chunks)
    hidden = lax.all_gather(hidden_half, "core", axis=1, tiled=True)
    out_part = jnp.dot(hidden, w_down, preferred_element_type=jnp.float32)
    out_full = lax.psum(out_part, "tensor")
    cot = (out_full - targets.astype(jnp.float32)).astype(jnp.bfloat16)

    a_out_part = jnp.dot(cot, proj_model[:, RANK:], preferred_element_type=jnp.float32)
    side = lax.psum(jnp.concatenate([a_in_part, a_out_part], axis=1), ("z", "core"))

    dh_part = lax.dot_general(cot, w_down, (((1,), (1,)), ((), ())), preferred_element_type=jnp.float32)
    dh_part = lax.psum_scatter(dh_part.reshape(total, n_core, width_h), "core", scatter_dimension=1, tiled=False)
    dh_l, dh_h = reduce_to_ends(dh_part, n_z, chunks)

    ph = lax.dynamic_slice_in_dim(proj_hidden, core * width_h, width_h, 0)

    def b_of(dh, gate, up, sig, act, hid):
        dgate = (dh * up * sig * (1.0 + gate * (1.0 - sig))).astype(jnp.bfloat16)
        dup = (dh * act).astype(jnp.bfloat16)
        return jnp.concatenate(
            [
                jnp.dot(dgate, ph[:, :RANK], preferred_element_type=jnp.float32),
                jnp.dot(dup, ph[:, RANK : 2 * RANK], preferred_element_type=jnp.float32),
                jnp.dot(hid, ph[:, 2 * RANK :], preferred_element_type=jnp.float32),
            ],
            axis=1,
        )

    b_l = b_of(dh_l, g_l, u_l, s_l, a_l, h_l)
    b_h = b_of(dh_h, g_h, u_h, s_h, a_h, h_h)
    is_low = z == 0
    is_high = z == n_z - 1
    b_mine = jnp.where(is_low, b_l, b_h)
    b_mine = lax.psum(b_mine, ("core", "tensor"))
    side_mine = lax.dynamic_slice_in_dim(side, jnp.where(is_low, 0, half), half, 0)
    a_in = side_mine[:, :RANK]
    a_out = side_mine[:, RANK:]
    ht = half // SEQ
    position = lax.iota(jnp.int32, half)
    member = ((position // SEQ)[:, None] == lax.iota(jnp.int32, ht)[None, :]).astype(jnp.float32)
    g_gate = jnp.einsum("ts,ti,tj->sij", member, a_in, b_mine[:, :RANK], precision=hi)
    g_up = jnp.einsum("ts,ti,tj->sij", member, a_in, b_mine[:, RANK : 2 * RANK], precision=hi)
    g_down = jnp.einsum("ts,ti,tj->sij", member, b_mine[:, 2 * RANK :], a_out, precision=hi)
    g_half = jnp.stack([g_gate, g_up, g_down], axis=1).reshape(ht, 3 * RANK * RANK)
    zeros = jnp.zeros_like(g_half)
    g_low = jnp.where(is_low, g_half, zeros)
    g_high = jnp.where(jnp.logical_and(is_high, jnp.logical_not(is_low)), g_half, zeros)
    grads = lax.psum(jnp.concatenate([g_low, g_high], axis=0), "z")
    return lax.dot_general(
        grads.astype(jnp.bfloat16),
        store,
        (((1,), (1,)), ((), ())),
        preferred_element_type=jnp.float32,
    )


def solution(mesh):
    n_dp = mesh.shape["dp"]
    n_t = mesh.shape["tensor"]
    devices = np.asarray(mesh.devices).reshape(n_dp // 2, 2, n_t)
    fine = Mesh(devices, ("z", "core", "tensor"))
    dp = ("z", "core")
    return jax.shard_map(
        local,
        mesh=fine,
        in_specs=(
            P(None, dp),
            P(dp, None, "tensor"),
            P("tensor", dp),
            P(None, dp),
            P(dp, None),
            P("tensor", None),
            P(dp + ("tensor",), None),
        ),
        out_specs=P(None, dp + ("tensor",)),
        check_vma=False,
    )
```

```python
import jax
import jax.numpy as jnp
import numpy as np
from jax import lax
from jax.sharding import Mesh, PartitionSpec as P

RANK = 64
SEQ = 128


def local(tokens, w_gate_up, w_down, targets, proj_model, proj_hidden, store):
    n_z = lax.axis_size("z")
    n_core = lax.axis_size("core")
    n_t = lax.axis_size("tensor")
    z = lax.axis_index("z")
    core = lax.axis_index("core")
    t_idx = lax.axis_index("tensor")
    total = tokens.shape[0]
    rows_z = total // n_z
    rows_t = total // n_t
    width_ff = w_down.shape[0]
    width_h = width_ff // n_core
    hi = lax.Precision.HIGHEST
    tests = total // SEQ

    def over_dp(part):
        part = lax.psum_scatter(part.reshape(total, n_core, width_h), "core", scatter_dimension=1, tiled=False)
        part = lax.psum_scatter(part.astype(jnp.bfloat16), "z", scatter_dimension=0, tiled=True)
        return part.astype(jnp.float32)

    a_in_part = jnp.dot(tokens, proj_model[:, :RANK], preferred_element_type=jnp.float32)
    gate = over_dp(jnp.dot(tokens, w_gate_up[:, 0, :], preferred_element_type=jnp.float32))
    up = over_dp(jnp.dot(tokens, w_gate_up[:, 1, :], preferred_element_type=jnp.float32))
    sig = jax.nn.sigmoid(gate)
    act = gate * sig
    hidden_loc = (act * up).astype(jnp.bfloat16)
    hidden = lax.all_gather(hidden_loc, "z", axis=0, tiled=True)
    hidden = lax.all_gather(hidden, "core", axis=1, tiled=True)
    out_part = jnp.dot(hidden, w_down, preferred_element_type=jnp.float32)
    out_rows = lax.psum_scatter(out_part, "tensor", scatter_dimension=0, tiled=True)
    tgt_rows = lax.dynamic_slice_in_dim(targets, t_idx * rows_t, rows_t, 0)
    cot_rows = (out_rows - tgt_rows.astype(jnp.float32)).astype(jnp.bfloat16)
    cot = lax.all_gather(cot_rows, "tensor", axis=0, tiled=True)

    a_out_part = jnp.dot(cot, proj_model[:, RANK:], preferred_element_type=jnp.float32)
    side = lax.psum(jnp.concatenate([a_in_part, a_out_part], axis=1), ("z", "core"))

    dh = over_dp(lax.dot_general(cot, w_down, (((1,), (1,)), ((), ())), preferred_element_type=jnp.float32))
    dgate = (dh * up * sig * (1.0 + gate * (1.0 - sig))).astype(jnp.bfloat16)
    dup = (dh * act).astype(jnp.bfloat16)
    ph = lax.dynamic_slice_in_dim(proj_hidden, core * width_h, width_h, 0)
    b_part = jnp.concatenate(
        [
            jnp.dot(dgate, ph[:, :RANK], preferred_element_type=jnp.float32),
            jnp.dot(dup, ph[:, RANK : 2 * RANK], preferred_element_type=jnp.float32),
            jnp.dot(hidden_loc, ph[:, 2 * RANK :], preferred_element_type=jnp.float32),
        ],
        axis=1,
    )
    b_sum = lax.psum(b_part, ("core", "tensor"))
    side_z = lax.dynamic_slice_in_dim(side, z * rows_z, rows_z, 0)
    a_in = side_z[:, :RANK]
    a_out = side_z[:, RANK:]
    position = z * rows_z + lax.iota(jnp.int32, rows_z)
    member = ((position // SEQ)[:, None] == lax.iota(jnp.int32, tests)[None, :]).astype(jnp.float32)
    g_gate = jnp.einsum("ts,ti,tj->sij", member, a_in, b_sum[:, :RANK], precision=hi)
    g_up = jnp.einsum("ts,ti,tj->sij", member, a_in, b_sum[:, RANK : 2 * RANK], precision=hi)
    g_down = jnp.einsum("ts,ti,tj->sij", member, b_sum[:, 2 * RANK :], a_out, precision=hi)
    grads = lax.psum(jnp.stack([g_gate, g_up, g_down], axis=1).reshape(tests, 3 * RANK * RANK), "z")
    return lax.dot_general(
        grads.astype(jnp.bfloat16),
        store,
        (((1,), (1,)), ((), ())),
        preferred_element_type=jnp.float32,
    )


def solution(mesh):
    n_dp = mesh.shape["dp"]
    n_t = mesh.shape["tensor"]
    devices = np.asarray(mesh.devices).reshape(n_dp // 2, 2, n_t)
    fine = Mesh(devices, ("z", "core", "tensor"))
    dp = ("z", "core")
    return jax.shard_map(
        local,
        mesh=fine,
        in_specs=(
            P(None, dp),
            P(dp, None, "tensor"),
            P("tensor", dp),
            P(None, dp),
            P(dp, None),
            P("tensor", None),
            P(dp + ("tensor",), None),
        ),
        out_specs=P(None, dp + ("tensor",)),
        check_vma=False,
    )
```

```python
import jax
import jax.numpy as jnp
from jax import lax
from jax.sharding import PartitionSpec as P

RANK = 64
SEQ = 128


def local(tokens, w_gate_up, w_down, targets, proj_model, proj_hidden, store):
    total = tokens.shape[0]
    hi = lax.Precision.HIGHEST
    tests = total // SEQ
    a_in_part = jnp.dot(tokens, proj_model[:, :RANK], preferred_element_type=jnp.float32)
    n_dp = lax.axis_size("dp")
    rows = total // n_dp
    width_ff = w_down.shape[0]
    both = jnp.einsum("td,dkf->ktf", tokens, w_gate_up, preferred_element_type=jnp.float32)
    both = both.astype(jnp.bfloat16).reshape(2, n_dp, rows, width_ff).transpose(1, 0, 2, 3)
    gate_up = lax.psum_scatter(
        both.reshape(n_dp * 2 * rows, width_ff), "dp", scatter_dimension=0, tiled=True
    ).astype(jnp.float32).reshape(2, rows, width_ff)
    gate = gate_up[0]
    up = gate_up[1]
    sig = jax.nn.sigmoid(gate)
    act = gate * sig
    hidden = (act * up).astype(jnp.bfloat16)
    out_part = jnp.dot(
        lax.all_gather(hidden, "dp", axis=0, tiled=True), w_down, preferred_element_type=jnp.float32
    )
    out_full = lax.psum(out_part, "tensor")
    cot = (out_full - targets.astype(jnp.float32)).astype(jnp.bfloat16)
    a_out_part = jnp.dot(cot, proj_model[:, RANK:], preferred_element_type=jnp.float32)
    side = lax.psum(jnp.concatenate([a_in_part, a_out_part], axis=1), "dp")
    grad_hidden = lax.psum_scatter(
        lax.dot_general(
            cot, w_down, (((1,), (1,)), ((), ())), preferred_element_type=jnp.float32
        ),
        "dp",
        scatter_dimension=0,
        tiled=True,
    )
    dgate = (grad_hidden * up * sig * (1.0 + gate * (1.0 - sig))).astype(jnp.bfloat16)
    dup = (grad_hidden * act).astype(jnp.bfloat16)
    hid_part = jnp.concatenate(
        [
            jnp.dot(dgate, proj_hidden[:, :RANK], preferred_element_type=jnp.float32),
            jnp.dot(dup, proj_hidden[:, RANK : 2 * RANK], preferred_element_type=jnp.float32),
            jnp.dot(hidden, proj_hidden[:, 2 * RANK :], preferred_element_type=jnp.float32),
        ],
        axis=1,
    )
    hid_sum = lax.all_gather(lax.psum(hid_part, "tensor"), "dp", axis=0, tiled=True)
    a_in = side[:, :RANK]
    a_out = side[:, RANK:]
    position = lax.iota(jnp.int32, total)
    member = ((position // SEQ)[:, None] == lax.iota(jnp.int32, tests)[None, :]).astype(jnp.float32)
    g_gate = jnp.einsum("ts,ti,tj->sij", member, a_in, hid_sum[:, :RANK], precision=hi)
    g_up = jnp.einsum("ts,ti,tj->sij", member, a_in, hid_sum[:, RANK : 2 * RANK], precision=hi)
    g_down = jnp.einsum("ts,ti,tj->sij", member, hid_sum[:, 2 * RANK :], a_out, precision=hi)
    grads = jnp.stack([g_gate, g_up, g_down], axis=1).reshape(tests, 3 * RANK * RANK)
    return lax.dot_general(
        grads.astype(jnp.bfloat16),
        store,
        (((1,), (1,)), ((), ())),
        preferred_element_type=jnp.float32,
    )


def solution(mesh):
    return jax.shard_map(
        local,
        mesh=mesh,
        in_specs=(
            P(None, "dp"),
            P("dp", None, "tensor"),
            P("tensor", "dp"),
            P(None, "dp"),
            P("dp", None),
            P("tensor", None),
            P(("dp", "tensor"), None),
        ),
        out_specs=P(None, ("dp", "tensor")),
        check_vma=False,
    )
```

```python
import jax
import jax.numpy as jnp
from jax import lax
import numpy as np
from jax.sharding import Mesh, PartitionSpec as P

RANK = 64
SEQ = 128
DP = ("z", "core")


def local(tokens, w_gate_up, w_down, targets, proj_model, proj_hidden, store):
    total = tokens.shape[0]
    hi = lax.Precision.HIGHEST
    tests = total // SEQ
    a_in_part = jnp.dot(tokens, proj_model[:, :RANK], preferred_element_type=jnp.float32)
    n_z = lax.axis_size("z")
    n_core = lax.axis_size("core")
    rows_z = total // n_z
    width_ff = w_down.shape[0]
    width_h = width_ff // n_core
    both = jnp.einsum("td,dkf->tkf", tokens, w_gate_up, preferred_element_type=jnp.float32)
    both = both.reshape(total, 2, n_core, width_h)
    both = lax.psum_scatter(both, "core", scatter_dimension=2, tiled=False)
    one = 1.0 + 0.0 * lax.axis_index("z").astype(jnp.float32)
    both = lax.psum_scatter(
        (both * one).astype(jnp.bfloat16), "z", scatter_dimension=0, tiled=True
    ).astype(jnp.float32)
    gate_up = lax.all_to_all(both, "core", 0, 2, tiled=True)
    gate = gate_up[:, 0]
    up = gate_up[:, 1]
    sig = jax.nn.sigmoid(gate)
    act = gate * sig
    hidden = (act * up).astype(jnp.bfloat16)
    out_part = jnp.dot(
        lax.all_gather(hidden, DP, axis=0, tiled=True), w_down, preferred_element_type=jnp.float32
    )
    out_full = lax.psum(out_part, "tensor")
    cot = (out_full - targets.astype(jnp.float32)).astype(jnp.bfloat16)
    a_out_part = jnp.dot(cot, proj_model[:, RANK:], preferred_element_type=jnp.float32)
    side = lax.psum(jnp.concatenate([a_in_part, a_out_part], axis=1), DP)
    grad_hidden = lax.psum_scatter(
        lax.dot_general(
            cot, w_down, (((1,), (1,)), ((), ())), preferred_element_type=jnp.float32
        ).astype(jnp.bfloat16),
        DP,
        scatter_dimension=0,
        tiled=True,
    ).astype(jnp.float32)
    dgate = (grad_hidden * up * sig * (1.0 + gate * (1.0 - sig))).astype(jnp.bfloat16)
    dup = (grad_hidden * act).astype(jnp.bfloat16)
    hid_part = jnp.concatenate(
        [
            jnp.dot(dgate, proj_hidden[:, :RANK], preferred_element_type=jnp.float32),
            jnp.dot(dup, proj_hidden[:, RANK : 2 * RANK], preferred_element_type=jnp.float32),
            jnp.dot(hidden, proj_hidden[:, 2 * RANK :], preferred_element_type=jnp.float32),
        ],
        axis=1,
    )
    hid_sum = lax.all_gather(lax.psum(hid_part, "tensor"), DP, axis=0, tiled=True)
    a_in = side[:, :RANK]
    a_out = side[:, RANK:]
    position = lax.iota(jnp.int32, total)
    member = ((position // SEQ)[:, None] == lax.iota(jnp.int32, tests)[None, :]).astype(jnp.float32)
    g_gate = jnp.einsum("ts,ti,tj->sij", member, a_in, hid_sum[:, :RANK], precision=hi)
    g_up = jnp.einsum("ts,ti,tj->sij", member, a_in, hid_sum[:, RANK : 2 * RANK], precision=hi)
    g_down = jnp.einsum("ts,ti,tj->sij", member, hid_sum[:, 2 * RANK :], a_out, precision=hi)
    grads = jnp.stack([g_gate, g_up, g_down], axis=1).reshape(tests, 3 * RANK * RANK)
    return lax.dot_general(
        grads.astype(jnp.bfloat16),
        store,
        (((1,), (1,)), ((), ())),
        preferred_element_type=jnp.float32,
    )


def solution(mesh):
    n_dp = mesh.shape["dp"]
    n_t = mesh.shape["tensor"]
    devices = np.asarray(mesh.devices).reshape(n_dp // 2, 2, n_t)
    fine = Mesh(devices, ("z", "core", "tensor"))
    return jax.shard_map(
        local,
        mesh=fine,
        in_specs=(
            P(None, DP),
            P(DP, None, "tensor"),
            P("tensor", DP),
            P(None, DP),
            P(DP, None),
            P("tensor", None),
            P(DP + ("tensor",), None),
        ),
        out_specs=P(None, DP + ("tensor",)),
        check_vma=False,
    )
```

```python
import jax
import jax.numpy as jnp
from jax import lax
from jax.sharding import PartitionSpec as P

RANK = 64
SEQ = 128


def local(tokens, w_gate_up, w_down, targets, proj_model, proj_hidden, store):
    total = tokens.shape[0]
    hi = lax.Precision.HIGHEST
    tests = total // SEQ
    a_in_part = jnp.dot(tokens, proj_model[:, :RANK], preferred_element_type=jnp.float32)
    both = jnp.einsum("td,dkf->ktf", tokens, w_gate_up, preferred_element_type=jnp.float32)
    gate = lax.psum_scatter(both[0], "dp", scatter_dimension=0, tiled=True)
    up = lax.psum_scatter(
        both[1].astype(jnp.bfloat16), "dp", scatter_dimension=0, tiled=True
    ).astype(jnp.float32)
    sig = jax.nn.sigmoid(gate)
    act = gate * sig
    hidden = (act * up).astype(jnp.bfloat16)
    out_part = jnp.dot(
        lax.all_gather(hidden, "dp", axis=0, tiled=True), w_down, preferred_element_type=jnp.float32
    )
    out_full = lax.psum(out_part, "tensor")
    cot = (out_full - targets.astype(jnp.float32)).astype(jnp.bfloat16)
    a_out_part = jnp.dot(cot, proj_model[:, RANK:], preferred_element_type=jnp.float32)
    side = lax.psum(jnp.concatenate([a_in_part, a_out_part], axis=1), "dp")
    grad_hidden = lax.psum_scatter(
        lax.dot_general(
            cot, w_down, (((1,), (1,)), ((), ())), preferred_element_type=jnp.float32
        ).astype(jnp.bfloat16),
        "dp",
        scatter_dimension=0,
        tiled=True,
    ).astype(jnp.float32)
    dgate = (grad_hidden * up * sig * (1.0 + gate * (1.0 - sig))).astype(jnp.bfloat16)
    dup = (grad_hidden * act).astype(jnp.bfloat16)
    hid_part = jnp.concatenate(
        [
            jnp.dot(dgate, proj_hidden[:, :RANK], preferred_element_type=jnp.float32),
            jnp.dot(dup, proj_hidden[:, RANK : 2 * RANK], preferred_element_type=jnp.float32),
            jnp.dot(hidden, proj_hidden[:, 2 * RANK :], preferred_element_type=jnp.float32),
        ],
        axis=1,
    )
    hid_sum = lax.all_gather(lax.psum(hid_part, "tensor"), "dp", axis=0, tiled=True)
    a_in = side[:, :RANK]
    a_out = side[:, RANK:]
    position = lax.iota(jnp.int32, total)
    member = ((position // SEQ)[:, None] == lax.iota(jnp.int32, tests)[None, :]).astype(jnp.float32)
    g_gate = jnp.einsum("ts,ti,tj->sij", member, a_in, hid_sum[:, :RANK], precision=hi)
    g_up = jnp.einsum("ts,ti,tj->sij", member, a_in, hid_sum[:, RANK : 2 * RANK], precision=hi)
    g_down = jnp.einsum("ts,ti,tj->sij", member, hid_sum[:, 2 * RANK :], a_out, precision=hi)
    grads = jnp.stack([g_gate, g_up, g_down], axis=1).reshape(tests, 3 * RANK * RANK)
    return lax.dot_general(
        grads.astype(jnp.bfloat16),
        store,
        (((1,), (1,)), ((), ())),
        preferred_element_type=jnp.float32,
    )


def solution(mesh):
    return jax.shard_map(
        local,
        mesh=mesh,
        in_specs=(
            P(None, "dp"),
            P("dp", None, "tensor"),
            P("tensor", "dp"),
            P(None, "dp"),
            P("dp", None),
            P("tensor", None),
            P(("dp", "tensor"), None),
        ),
        out_specs=P(None, ("dp", "tensor")),
        check_vma=False,
    )
```
